128 devices in a mesh: rows: 32 (over x, y, core), dims: 4 (over z).
Axes of the slice: x: 4, y: 4, z: 4, core: 2. Of those that a mesh axis runs over, the one named last changes fastest.
Arguments:
- gradients: float32 [65536, 4096], P('rows', 'dims'), may hold values from -0.5 to 0.5
- ridge: float32 [], replicated, may hold values from 2 to 8
- panel_index: int32 [1], replicated, may hold values from 0 to 63
- block_ids: int32 [64], replicated, may hold values from 0 to 63, each once
Outputs:
- panel: float32 [65536, 1024], P(('rows', 'dims'))
The draws below stay inside these ranges and needn't reach their ends.
Inputs may be any that keep to these rules, and one draw needn't show every extreme that they name: block_ids is a permutation of the row blocks' numbers.
All inputs are finite; a program needn't handle non-finite values.
Results may differ from the reference program's by a relative error of at most 0.000081.
Values sent between devices are 32-bit elements; how exact they have to be, the bound alone decides.
No kernel may reach another device: no remote copies, remote signals or barrier semaphores. Data moves between devices by JAX's collectives and lax.ppermute only.
A program may use at most 128 MiB of HBM per device.

```python
import jax
import jax.numpy as jnp
from jax import lax

D = 4096
B = 1024
BLOCKS = 64
EXAMPLES = 65536


def steps_of(rng, dims, shards, least, largest):
    level = 1.0
    for dim, blocks in shards:
        heights = jax.random.uniform(jax.random.fold_in(jax.random.fold_in(rng, 6), dim), (blocks,), jnp.float32, least / len(shards), largest / len(shards))
        level = level * jnp.repeat(jnp.exp(heights), dims[dim] // blocks).reshape((-1,) + (1,) * (len(dims) - 1 - dim))
    return level


def scatter_about(stream_key, shape, scale, most, pieces=(), held_as=jnp.bfloat16):
    drawn = scale * jax.random.normal(stream_key, shape, jnp.float32)
    if pieces:
        drawn = drawn * steps_of(stream_key, shape, pieces, -0.22, 0.18)
    return jnp.clip(drawn, -most, most).astype(held_as)


def setup_inputs(seed: int = 0) -> dict:
    key_of = jax.random.split(jax.random.key(seed), 5)
    return {
        "gradients": scatter_about(key_of[0], (EXAMPLES, D), 0.0625, 0.5, ((0, 32), (1, 4)), jnp.float32),
        "ridge": jnp.clip(jax.random.uniform(key_of[1], (), jnp.float32, 2.0, 8.0), 2.0, 8.0),
        "panel_index": jax.random.randint(key_of[2], (1,), 0, BLOCKS).astype(jnp.int32),
        "block_ids": jax.random.permutation(key_of[3], BLOCKS).astype(jnp.int32),
    }


def reference(gradients, ridge, panel_index, block_ids):
    ids = jnp.arange(BLOCKS, dtype=jnp.int32)
    position = jnp.sum(jnp.where(block_ids == panel_index[0], ids, 0)).astype(jnp.int32)
    pivot = lax.dynamic_slice_in_dim(gradients, (position * B).astype(jnp.int32), B, 0)
    column = lax.dot_general(gradients.astype(jnp.float32), pivot.astype(jnp.float32), (((1,), (1,)), ((), ())), precision=lax.Precision.HIGHEST, preferred_element_type=jnp.float32)
    row_ids = jnp.arange(EXAMPLES, dtype=jnp.int32)[:, None]
    col_ids = position * B + jnp.arange(B, dtype=jnp.int32)[None, :]
    column = column + jnp.where(row_ids == col_ids, ridge, jnp.float32(0.0))
    tile = lax.dot_general(pivot.astype(jnp.float32), pivot.astype(jnp.float32), (((1,), (1,)), ((), ())), precision=lax.Precision.HIGHEST, preferred_element_type=jnp.float32)
    factor = jnp.linalg.cholesky(tile + ridge * jnp.eye(B, dtype=jnp.float32))
    return lax.linalg.triangular_solve(factor, column, left_side=False, lower=True, transpose_a=True)
```

```python
import jax
import jax.numpy as jnp
from jax import lax
from jax.sharding import PartitionSpec as P

B = 1024


def broadcast(array, axis, root):
    mine = lax.axis_index(axis) == root
    return lax.psum(jnp.where(mine, array, jnp.zeros_like(array)), axis)


def per_device(gradients, ridge, panel_index, block_ids):
    local_rows = gradients.shape[0]
    blocks_here = local_rows // B
    ids = jnp.arange(block_ids.shape[0], dtype=jnp.int32)
    position = jnp.sum(jnp.where(block_ids == panel_index[0], ids, 0))
    owner = position // blocks_here
    offset = position % blocks_here * B
    own_tile = lax.dynamic_slice_in_dim(gradients, offset, B, 0)
    pivot = broadcast(own_tile, "rows", owner)
    numbers = (((1,), (1,)), ((), ()))
    share = local_rows // lax.axis_size("dims")

    rows_n = lax.axis_size("rows")
    core = lax.axis_index("rows") % 2
    half = B // 2
    mine = lax.dynamic_slice_in_dim(pivot, core * half, half, 0)
    tile_half = lax.psum(
        lax.dot_general(
            mine, pivot, numbers, precision=lax.Precision.HIGHEST, preferred_element_type=jnp.float32
        ),
        "dims",
    )
    other_half = lax.ppermute(tile_half, "rows", [(i, i ^ 1) for i in range(rows_n)])
    tile = jnp.where(
        core == 0,
        jnp.concatenate([tile_half, other_half], axis=0),
        jnp.concatenate([other_half, tile_half], axis=0),
    )

    column = lax.psum_scatter(
        lax.dot_general(
            gradients,
            pivot,
            numbers,
            precision=lax.Precision.HIGHEST,
            preferred_element_type=jnp.float32,
        ),
        "dims",
        scatter_dimension=0,
        tiled=True,
    )
    first = lax.axis_index("rows") * local_rows + lax.axis_index("dims") * share
    row_ids = first + jnp.arange(share, dtype=jnp.int32)[:, None]
    col_ids = position * B + jnp.arange(B, dtype=jnp.int32)[None, :]
    column = column + jnp.where(row_ids == col_ids, ridge, jnp.float32(0.0))
    factor = jnp.linalg.cholesky(tile + ridge * jnp.eye(B, dtype=jnp.float32))
    return lax.linalg.triangular_solve(
        factor, column, left_side=False, lower=True, transpose_a=True
    )


def solution(mesh):
    in_specs = (P("rows", "dims"), P(), P(), P())
    out_specs = P(("rows", "dims"), None)
    return jax.shard_map(
        per_device, mesh=mesh, in_specs=in_specs, out_specs=out_specs, check_vma=False
    )
```

```python
import jax
import jax.numpy as jnp
from jax import lax
from jax.experimental import pallas as pl
from jax.experimental.pallas import tpu as pltpu
from jax.sharding import PartitionSpec as P

NB = 128
HI = lax.Precision.HIGHEST


def _dot_t(a, b):
    return lax.dot_general(a, b, (((1,), (1,)), ((), ())), precision=HI, preferred_element_type=jnp.float32)


def _dot(a, b):
    return lax.dot_general(a, b, (((1,), (0,)), ((), ())), precision=HI, preferred_element_type=jnp.float32)


def _inv_chol_kernel(a_ref, w_ref, work):
    n = a_ref.shape[0]
    nblk = n // NB
    work[...] = a_ref[...]
    w_ref[...] = jnp.zeros_like(w_ref)
    rid = lax.broadcasted_iota(jnp.int32, (NB, NB), 0)
    cid = lax.broadcasted_iota(jnp.int32, (NB, NB), 1)
    rid1 = lax.broadcasted_iota(jnp.int32, (NB, 1), 0)
    cid1 = lax.broadcasted_iota(jnp.int32, (1, NB), 1)
    eye = jnp.where(rid == cid, 1.0, 0.0).astype(jnp.float32)

    def step(k, carry):
        s, r = carry
        row = jnp.sum(jnp.where(rid == k, s, 0.0), axis=0, keepdims=True)
        col = jnp.sum(jnp.where(cid == k, s, 0.0), axis=1, keepdims=True)
        d = jnp.sum(jnp.where(cid1 == k, row, 0.0), axis=1, keepdims=True)
        inv = 1.0 / jnp.sqrt(d)
        l_row = jnp.where(cid1 >= k, row * inv, 0.0)
        l_col = jnp.where(rid1 >= k, col * inv, 0.0)
        s = s - l_col * l_row
        w_row = jnp.sum(jnp.where(rid == k, r, 0.0), axis=0, keepdims=True) * inv
        below = jnp.where(rid1 > k, l_col, 0.0)
        r = jnp.where(rid == k, w_row, r - below * w_row)
        return s, r

    for j in range(nblk):
        o = j * NB
        s = work[o:o + NB, o:o + NB]
        _, wjj = lax.fori_loop(0, NB, step, (s, eye))
        w_ref[o:o + NB, o:o + NB] = wjj
        if j < nblk - 1:
            lij = _dot_t(work[o + NB:, o:o + NB], wjj)
            work[o + NB:, o:o + NB] = lij
            work[o + NB:, o + NB:] = work[o + NB:, o + NB:] - _dot_t(lij, lij)
    for i in range(1, nblk):
        o = i * NB
        t = _dot(work[o:o + NB, 0:o], w_ref[0:o, 0:o])
        w_ref[o:o + NB, 0:o] = -_dot(w_ref[o:o + NB, o:o + NB], t)


def inv_chol(a):
    n = a.shape[0]
    return pl.pallas_call(
        _inv_chol_kernel,
        out_shape=jax.ShapeDtypeStruct((n, n), jnp.float32),
        in_specs=[pl.BlockSpec(memory_space=pltpu.VMEM)],
        out_specs=pl.BlockSpec(memory_space=pltpu.VMEM),
        scratch_shapes=[pltpu.VMEM((n, n), jnp.float32)],
    )(a)


B = 1024


def broadcast(array, axis, root):
    mine = lax.axis_index(axis) == root
    return lax.psum(jnp.where(mine, array, jnp.zeros_like(array)), axis)


def per_device(gradients, ridge, panel_index, block_ids):
    local_rows = gradients.shape[0]
    blocks_here = local_rows // B
    ids = jnp.arange(block_ids.shape[0], dtype=jnp.int32)
    position = jnp.sum(jnp.where(block_ids == panel_index[0], ids, 0))
    owner = position // blocks_here
    offset = position % blocks_here * B
    own_tile = lax.dynamic_slice_in_dim(gradients, offset, B, 0)
    pivot = broadcast(own_tile, "rows", owner)
    numbers = (((1,), (1,)), ((), ()))
    share = local_rows // lax.axis_size("dims")

    rows_n = lax.axis_size("rows")
    core = lax.axis_index("rows") % 2
    half = B // 2
    mine = lax.dynamic_slice_in_dim(pivot, core * half, half, 0)
    tile_half = lax.psum(
        lax.dot_general(
            mine, pivot, numbers, precision=lax.Precision.HIGHEST, preferred_element_type=jnp.float32
        ),
        "dims",
    )
    other_half = lax.ppermute(tile_half, "rows", [(i, i ^ 1) for i in range(rows_n)])
    tile = jnp.where(
        core == 0,
        jnp.concatenate([tile_half, other_half], axis=0),
        jnp.concatenate([other_half, tile_half], axis=0),
    )

    column = lax.psum_scatter(
        lax.dot_general(
            gradients,
            pivot,
            numbers,
            precision=lax.Precision.HIGHEST,
            preferred_element_type=jnp.float32,
        ),
        "dims",
        scatter_dimension=0,
        tiled=True,
    )
    first = lax.axis_index("rows") * local_rows + lax.axis_index("dims") * share
    row_ids = first + jnp.arange(share, dtype=jnp.int32)[:, None]
    col_ids = position * B + jnp.arange(B, dtype=jnp.int32)[None, :]
    column = column + jnp.where(row_ids == col_ids, ridge, jnp.float32(0.0))
    inverse = inv_chol(tile + ridge * jnp.eye(B, dtype=jnp.float32))
    return _dot_t(column, inverse)


def solution(mesh):
    in_specs = (P("rows", "dims"), P(), P(), P())
    out_specs = P(("rows", "dims"), None)
    return jax.shard_map(
        per_device, mesh=mesh, in_specs=in_specs, out_specs=out_specs, check_vma=False
    )
```

```python
import jax
import jax.numpy as jnp
from jax import lax
from jax.experimental import pallas as pl
from jax.experimental.pallas import tpu as pltpu
from jax.sharding import PartitionSpec as P

NB = 128
HI = lax.Precision.HIGHEST


def _dot_t(a, b):
    return lax.dot_general(a, b, (((1,), (1,)), ((), ())), precision=HI, preferred_element_type=jnp.float32)


def _dot(a, b):
    return lax.dot_general(a, b, (((1,), (0,)), ((), ())), precision=HI, preferred_element_type=jnp.float32)


def _inv_chol_kernel(a_ref, w_ref, work):
    n = a_ref.shape[0]
    nblk = n // NB
    work[...] = a_ref[...]
    w_ref[...] = jnp.zeros_like(w_ref)
    rid = lax.broadcasted_iota(jnp.int32, (NB, NB), 0)
    cid = lax.broadcasted_iota(jnp.int32, (NB, NB), 1)
    rid1 = lax.broadcasted_iota(jnp.int32, (NB, 1), 0)
    cid1 = lax.broadcasted_iota(jnp.int32, (1, NB), 1)
    eye = jnp.where(rid == cid, 1.0, 0.0).astype(jnp.float32)

    def step(k, carry):
        s, r = carry
        row = jnp.sum(jnp.where(rid == k, s, 0.0), axis=0, keepdims=True)
        col = jnp.sum(jnp.where(cid == k, s, 0.0), axis=1, keepdims=True)
        d = jnp.sum(jnp.where(rid1 == k, col, 0.0), axis=0, keepdims=True)
        inv = lax.rsqrt(d)
        l_row = jnp.where(cid1 >= k, row * inv, 0.0)
        l_col = jnp.where(rid1 >= k, col * inv, 0.0)
        s = s - l_col * l_row
        w_row = jnp.sum(jnp.where(rid == k, r, 0.0), axis=0, keepdims=True) * inv
        below = jnp.where(rid1 > k, l_col, 0.0)
        r = jnp.where(rid == k, w_row, r - below * w_row)
        return s, r

    for j in range(nblk):
        o = j * NB
        s = work[o:o + NB, o:o + NB]
        _, wjj = lax.fori_loop(0, NB, step, (s, eye), unroll=8)
        w_ref[o:o + NB, o:o + NB] = wjj
        if j < nblk - 1:
            lij = _dot_t(work[o + NB:, o:o + NB], wjj)
            work[o + NB:, o:o + NB] = lij
            work[o + NB:, o + NB:] = work[o + NB:, o + NB:] - _dot_t(lij, lij)
    for i in range(1, nblk):
        o = i * NB
        t = _dot(work[o:o + NB, 0:o], w_ref[0:o, 0:o])
        w_ref[o:o + NB, 0:o] = -_dot(w_ref[o:o + NB, o:o + NB], t)


def inv_chol(a):
    n = a.shape[0]
    return pl.pallas_call(
        _inv_chol_kernel,
        out_shape=jax.ShapeDtypeStruct((n, n), jnp.float32),
        in_specs=[pl.BlockSpec(memory_space=pltpu.VMEM)],
        out_specs=pl.BlockSpec(memory_space=pltpu.VMEM),
        scratch_shapes=[pltpu.VMEM((n, n), jnp.float32)],
    )(a)


B = 1024


def broadcast(array, axis, root):
    mine = lax.axis_index(axis) == root
    return lax.psum(jnp.where(mine, array, jnp.zeros_like(array)), axis)


def per_device(gradients, ridge, panel_index, block_ids):
    local_rows = gradients.shape[0]
    blocks_here = local_rows // B
    ids = jnp.arange(block_ids.shape[0], dtype=jnp.int32)
    position = jnp.sum(jnp.where(block_ids == panel_index[0], ids, 0))
    owner = position // blocks_here
    offset = position % blocks_here * B
    own_tile = lax.dynamic_slice_in_dim(gradients, offset, B, 0)
    pivot = broadcast(own_tile, "rows", owner)
    numbers = (((1,), (1,)), ((), ()))
    share = local_rows // lax.axis_size("dims")

    rows_n = lax.axis_size("rows")
    core = lax.axis_index("rows") % 2
    half = B // 2
    mine = lax.dynamic_slice_in_dim(pivot, core * half, half, 0)
    tile_half = lax.psum(
        lax.dot_general(
            mine, pivot, numbers, precision=lax.Precision.HIGHEST, preferred_element_type=jnp.float32
        ),
        "dims",
    )
    other_half = lax.ppermute(tile_half, "rows", [(i, i ^ 1) for i in range(rows_n)])
    tile = jnp.where(
        core == 0,
        jnp.concatenate([tile_half, other_half], axis=0),
        jnp.concatenate([other_half, tile_half], axis=0),
    )

    column = lax.psum_scatter(
        lax.dot_general(
            gradients,
            pivot,
            numbers,
            precision=lax.Precision.HIGHEST,
            preferred_element_type=jnp.float32,
        ),
        "dims",
        scatter_dimension=0,
        tiled=True,
    )
    first = lax.axis_index("rows") * local_rows + lax.axis_index("dims") * share
    row_ids = first + jnp.arange(share, dtype=jnp.int32)[:, None]
    col_ids = position * B + jnp.arange(B, dtype=jnp.int32)[None, :]
    column = column + jnp.where(row_ids == col_ids, ridge, jnp.float32(0.0))
    inverse = inv_chol(tile + ridge * jnp.eye(B, dtype=jnp.float32))
    return _dot_t(column, inverse)


def solution(mesh):
    in_specs = (P("rows", "dims"), P(), P(), P())
    out_specs = P(("rows", "dims"), None)
    return jax.shard_map(
        per_device, mesh=mesh, in_specs=in_specs, out_specs=out_specs, check_vma=False
    )
```

```python
import jax
import jax.numpy as jnp
from jax import lax
from jax.experimental import pallas as pl
from jax.experimental.pallas import tpu as pltpu
from jax.sharding import PartitionSpec as P

NB = 128
HI = lax.Precision.HIGHEST


def _dot_t(a, b):
    return lax.dot_general(a, b, (((1,), (1,)), ((), ())), precision=HI, preferred_element_type=jnp.float32)


def _dot_high(a, b):
    return lax.dot_general(
        a, b, (((1,), (1,)), ((), ())), precision=lax.Precision.HIGH, preferred_element_type=jnp.float32
    )


def _dot(a, b):
    return lax.dot_general(a, b, (((1,), (0,)), ((), ())), precision=HI, preferred_element_type=jnp.float32)


def _inv_chol_kernel(a_ref, w_ref, work):
    n = a_ref.shape[0]
    nblk = n // NB
    work[...] = a_ref[...]
    w_ref[...] = jnp.zeros_like(w_ref)
    rid = lax.broadcasted_iota(jnp.int32, (NB, NB), 0)
    cid = lax.broadcasted_iota(jnp.int32, (NB, NB), 1)
    rid1 = lax.broadcasted_iota(jnp.int32, (NB, 1), 0)
    cid1 = lax.broadcasted_iota(jnp.int32, (1, NB), 1)
    eye = jnp.where(rid == cid, 1.0, 0.0).astype(jnp.float32)

    def step(k, carry):
        s, r = carry
        row = jnp.sum(jnp.where(rid == k, s, 0.0), axis=0, keepdims=True)
        col = jnp.sum(jnp.where(cid == k, s, 0.0), axis=1, keepdims=True)
        d = jnp.sum(jnp.where(rid1 == k, col, 0.0), axis=0, keepdims=True)
        inv = lax.rsqrt(d)
        l_row = jnp.where(cid1 >= k, row * inv, 0.0)
        l_col = jnp.where(rid1 >= k, col * inv, 0.0)
        s = s - l_col * l_row
        w_row = jnp.sum(jnp.where(rid == k, r, 0.0), axis=0, keepdims=True) * inv
        below = jnp.where(rid1 > k, l_col, 0.0)
        r = jnp.where(rid == k, w_row, r - below * w_row)
        return s, r

    for j in range(nblk):
        o = j * NB
        s = work[o:o + NB, o:o + NB]
        _, wjj = lax.fori_loop(0, NB, step, (s, eye), unroll=8)
        w_ref[o:o + NB, o:o + NB] = wjj
        if j < nblk - 1:
            lij = _dot_t(work[o + NB:, o:o + NB], wjj)
            work[o + NB:, o:o + NB] = lij
            work[o + NB:, o + NB:] = work[o + NB:, o + NB:] - _dot_t(lij, lij)
    for i in range(1, nblk):
        o = i * NB
        t = _dot(work[o:o + NB, 0:o], w_ref[0:o, 0:o])
        w_ref[o:o + NB, 0:o] = -_dot(w_ref[o:o + NB, o:o + NB], t)


def inv_chol(a):
    n = a.shape[0]
    return pl.pallas_call(
        _inv_chol_kernel,
        out_shape=jax.ShapeDtypeStruct((n, n), jnp.float32),
        in_specs=[pl.BlockSpec(memory_space=pltpu.VMEM)],
        out_specs=pl.BlockSpec(memory_space=pltpu.VMEM),
        scratch_shapes=[pltpu.VMEM((n, n), jnp.float32)],
    )(a)


B = 1024


def broadcast(array, axis, root):
    mine = lax.axis_index(axis) == root
    return lax.psum(jnp.where(mine, array, jnp.zeros_like(array)), axis)


def per_device(gradients, ridge, panel_index, block_ids):
    local_rows = gradients.shape[0]
    blocks_here = local_rows // B
    ids = jnp.arange(block_ids.shape[0], dtype=jnp.int32)
    position = jnp.sum(jnp.where(block_ids == panel_index[0], ids, 0))
    owner = position // blocks_here
    offset = position % blocks_here * B
    own_tile = lax.dynamic_slice_in_dim(gradients, offset, B, 0)
    pivot = broadcast(own_tile, "rows", owner)
    numbers = (((1,), (1,)), ((), ()))
    share = local_rows // lax.axis_size("dims")

    rows_n = lax.axis_size("rows")
    core = lax.axis_index("rows") % 2
    half = B // 2
    mine = lax.dynamic_slice_in_dim(pivot, core * half, half, 0)
    tile_half = lax.psum(
        lax.dot_general(
            mine, pivot, numbers, precision=lax.Precision.HIGH, preferred_element_type=jnp.float32
        ),
        "dims",
    )
    other_half = lax.ppermute(tile_half, "rows", [(i, i ^ 1) for i in range(rows_n)])
    tile = jnp.where(
        core == 0,
        jnp.concatenate([tile_half, other_half], axis=0),
        jnp.concatenate([other_half, tile_half], axis=0),
    )

    column = lax.psum_scatter(
        lax.dot_general(
            gradients,
            pivot,
            numbers,
            precision=lax.Precision.HIGH,
            preferred_element_type=jnp.float32,
        ),
        "dims",
        scatter_dimension=0,
        tiled=True,
    )
    first = lax.axis_index("rows") * local_rows + lax.axis_index("dims") * share
    row_ids = first + jnp.arange(share, dtype=jnp.int32)[:, None]
    col_ids = position * B + jnp.arange(B, dtype=jnp.int32)[None, :]
    column = column + jnp.where(row_ids == col_ids, ridge, jnp.float32(0.0))
    inverse = inv_chol(tile + ridge * jnp.eye(B, dtype=jnp.float32))
    return _dot_high(column, inverse)


def solution(mesh):
    in_specs = (P("rows", "dims"), P(), P(), P())
    out_specs = P(("rows", "dims"), None)
    return jax.shard_map(
        per_device, mesh=mesh, in_specs=in_specs, out_specs=out_specs, check_vma=False
    )
```

```python
import jax
import jax.numpy as jnp
from jax import lax
from jax.experimental import pallas as pl
from jax.experimental.pallas import tpu as pltpu
from jax.sharding import PartitionSpec as P

NB = 128
HI = lax.Precision.HIGHEST


def _dot_t(a, b):
    return lax.dot_general(a, b, (((1,), (1,)), ((), ())), precision=HI, preferred_element_type=jnp.float32)


def _dot_high(a, b):
    return lax.dot_general(
        a, b, (((1,), (1,)), ((), ())), precision=lax.Precision.HIGH, preferred_element_type=jnp.float32
    )


def _dot(a, b):
    return lax.dot_general(a, b, (((1,), (0,)), ((), ())), precision=HI, preferred_element_type=jnp.float32)


def _inv_chol_kernel(a_ref, w_ref, work):
    n = a_ref.shape[0]
    nblk = n // NB
    work[...] = a_ref[...]
    w_ref[...] = jnp.zeros_like(w_ref)
    rid = lax.broadcasted_iota(jnp.int32, (NB, NB), 0)
    cid = lax.broadcasted_iota(jnp.int32, (NB, NB), 1)
    rid1 = lax.broadcasted_iota(jnp.int32, (NB, 1), 0)
    cid1 = lax.broadcasted_iota(jnp.int32, (1, NB), 1)
    eye = jnp.where(rid == cid, 1.0, 0.0).astype(jnp.float32)

    def step(k, carry):
        s, r = carry
        row = jnp.sum(jnp.where(rid == k, s, 0.0), axis=0, keepdims=True)
        col = jnp.sum(jnp.where(cid == k, s, 0.0), axis=1, keepdims=True)
        d = jnp.sum(jnp.where(rid1 == k, col, 0.0), axis=0, keepdims=True)
        inv = lax.rsqrt(d)
        l_row = jnp.where(cid1 >= k, row * inv, 0.0)
        l_col = jnp.where(rid1 >= k, col * inv, 0.0)
        s = s - l_col * l_row
        w_row = jnp.sum(jnp.where(rid == k, r, 0.0), axis=0, keepdims=True) * inv
        below = jnp.where(rid1 > k, l_col, 0.0)
        r = jnp.where(rid == k, w_row, r - below * w_row)
        return s, r

    for j in range(nblk):
        o = j * NB
        s = work[o:o + NB, o:o + NB]
        _, wjj = lax.fori_loop(0, NB, step, (s, eye), unroll=8)
        w_ref[o:o + NB, o:o + NB] = wjj
        if j < nblk - 1:
            lij = _dot_t(work[o + NB:, o:o + NB], wjj)
            work[o + NB:, o:o + NB] = lij
            work[o + NB:, o + NB:] = work[o + NB:, o + NB:] - _dot_t(lij, lij)
    for i in range(1, nblk):
        o = i * NB
        t = _dot(work[o:o + NB, 0:o], w_ref[0:o, 0:o])
        w_ref[o:o + NB, 0:o] = -_dot(w_ref[o:o + NB, o:o + NB], t)


def inv_chol(a):
    n = a.shape[0]
    return pl.pallas_call(
        _inv_chol_kernel,
        out_shape=jax.ShapeDtypeStruct((n, n), jnp.float32),
        in_specs=[pl.BlockSpec(memory_space=pltpu.VMEM)],
        out_specs=pl.BlockSpec(memory_space=pltpu.VMEM),
        scratch_shapes=[pltpu.VMEM((n, n), jnp.float32)],
    )(a)


B = 1024


def broadcast(array, axis, root):
    mine = lax.axis_index(axis) == root
    return lax.psum(jnp.where(mine, array, jnp.zeros_like(array)), axis)


def per_device(gradients, ridge, panel_index, block_ids):
    local_rows = gradients.shape[0]
    blocks_here = local_rows // B
    ids = jnp.arange(block_ids.shape[0], dtype=jnp.int32)
    position = jnp.sum(jnp.where(block_ids == panel_index[0], ids, 0))
    owner = position // blocks_here
    offset = position % blocks_here * B
    own_tile = lax.dynamic_slice_in_dim(gradients, offset, B, 0)
    pivot = broadcast(own_tile, "rows", owner)
    numbers = (((1,), (1,)), ((), ()))
    share = local_rows // lax.axis_size("dims")

    rows_n = lax.axis_size("rows")
    core = lax.axis_index("rows") % 2
    half = B // 2
    r_ids = lax.broadcasted_iota(jnp.int32, (half, half), 0)
    c_ids = lax.broadcasted_iota(jnp.int32, (half, half), 1)
    top, bottom = pivot[:half], pivot[half:]

    def lower_left():
        x = _dot_high(bottom, top)
        return jnp.concatenate([x, jnp.zeros((8, half), jnp.float32)], axis=0)

    def diagonal_pair():
        t00 = _dot_high(top, top)
        t11 = _dot_high(bottom, bottom)
        m = jnp.where(r_ids >= c_ids, t00, t11)
        d11 = jnp.sum(jnp.where(r_ids == c_ids, t11, 0.0), axis=0, keepdims=True)
        return jnp.concatenate([m, jnp.broadcast_to(d11, (8, half))], axis=0)

    reduced = lax.psum(lax.cond(core == 0, lower_left, diagonal_pair), "dims")
    swapped = lax.ppermute(reduced, "rows", [(i, i ^ 1) for i in range(rows_n)])
    quarter_x = jnp.where(core == 0, reduced, swapped)[:half]
    packed = jnp.where(core == 0, swapped, reduced)
    m, d11 = packed[:half], packed[half:half + 1]
    t00 = jnp.where(r_ids >= c_ids, m, m.T)
    t11 = jnp.where(r_ids < c_ids, m, jnp.where(r_ids > c_ids, m.T, d11))
    tile = jnp.concatenate(
        [
            jnp.concatenate([t00, jnp.zeros((half, half), jnp.float32)], axis=1),
            jnp.concatenate([quarter_x, t11], axis=1),
        ],
        axis=0,
    )

    column = lax.psum_scatter(
        lax.dot_general(
            gradients,
            pivot,
            numbers,
            precision=lax.Precision.HIGH,
            preferred_element_type=jnp.float32,
        ),
        "dims",
        scatter_dimension=0,
        tiled=True,
    )
    first = lax.axis_index("rows") * local_rows + lax.axis_index("dims") * share
    row_ids = first + jnp.arange(share, dtype=jnp.int32)[:, None]
    col_ids = position * B + jnp.arange(B, dtype=jnp.int32)[None, :]
    column = column + jnp.where(row_ids == col_ids, ridge, jnp.float32(0.0))
    inverse = inv_chol(tile + ridge * jnp.eye(B, dtype=jnp.float32))
    return _dot_high(column, inverse)


def solution(mesh):
    in_specs = (P("rows", "dims"), P(), P(), P())
    out_specs = P(("rows", "dims"), None)
    return jax.shard_map(
        per_device, mesh=mesh, in_specs=in_specs, out_specs=out_specs, check_vma=False
    )
```

```python
import jax
import jax.numpy as jnp
from jax import lax
from jax.experimental import pallas as pl
from jax.experimental.pallas import tpu as pltpu
from jax.sharding import PartitionSpec as P

NB = 128
NPH = 8
HI = lax.Precision.HIGHEST


def _dot_t(a, b):
    return lax.dot_general(a, b, (((1,), (1,)), ((), ())), precision=HI, preferred_element_type=jnp.float32)


def _dot_high(a, b):
    return lax.dot_general(
        a, b, (((1,), (1,)), ((), ())), precision=lax.Precision.HIGH, preferred_element_type=jnp.float32
    )


def _dot(a, b):
    return lax.dot_general(a, b, (((1,), (0,)), ((), ())), precision=HI, preferred_element_type=jnp.float32)


def _factor_block(s):
    sub = NB // NPH
    cid1 = lax.broadcasted_iota(jnp.int32, (1, NB), 1)
    r = jnp.where(lax.broadcasted_iota(jnp.int32, (NB, NB), 0) == lax.broadcasted_iota(jnp.int32, (NB, NB), 1), 1.0, 0.0).astype(jnp.float32)
    done = []
    for p in range(NPH):
        base = p * sub
        rid1 = lax.broadcasted_iota(jnp.int32, (NB - base, 1), 0) + base

        def step(k, carry, rid1=rid1):
            s, r = carry
            row = jnp.sum(jnp.where(rid1 == k, s, 0.0), axis=0, keepdims=True)
            col = jnp.sum(jnp.where(cid1 == k, s, 0.0), axis=1, keepdims=True)
            d = jnp.sum(jnp.where(rid1 == k, col, 0.0), axis=0, keepdims=True)
            inv = lax.rsqrt(d)
            l_row = jnp.where(cid1 >= k, row * inv, 0.0)
            l_col = jnp.where(rid1 >= k, col * inv, 0.0)
            s = s - l_col * l_row
            w_row = jnp.sum(jnp.where(rid1 == k, r, 0.0), axis=0, keepdims=True) * inv
            below = jnp.where(rid1 > k, l_col, 0.0)
            r = jnp.where(rid1 == k, w_row, r - below * w_row)
            return s, r

        s, r = lax.fori_loop(base, base + sub, step, (s, r), unroll=True)
        done.append(r[:sub])
        s, r = s[sub:], r[sub:]
    return jnp.concatenate(done, axis=0)


def _inv_chol_kernel(a_ref, w_ref, work):
    n = a_ref.shape[0]
    nblk = n // NB
    work[...] = a_ref[...]
    w_ref[...] = jnp.zeros_like(w_ref)
    for j in range(nblk):
        o = j * NB
        wjj = _factor_block(work[o:o + NB, o:o + NB])
        w_ref[o:o + NB, o:o + NB] = wjj
        if j < nblk - 1:
            lij = _dot_t(work[o + NB:, o:o + NB], wjj)
            work[o + NB:, o:o + NB] = lij
            work[o + NB:, o + NB:] = work[o + NB:, o + NB:] - _dot_t(lij, lij)
    for i in range(1, nblk):
        o = i * NB
        t = _dot(work[o:o + NB, 0:o], w_ref[0:o, 0:o])
        w_ref[o:o + NB, 0:o] = -_dot(w_ref[o:o + NB, o:o + NB], t)


def inv_chol(a):
    n = a.shape[0]
    return pl.pallas_call(
        _inv_chol_kernel,
        out_shape=jax.ShapeDtypeStruct((n, n), jnp.float32),
        in_specs=[pl.BlockSpec(memory_space=pltpu.VMEM)],
        out_specs=pl.BlockSpec(memory_space=pltpu.VMEM),
        scratch_shapes=[pltpu.VMEM((n, n), jnp.float32)],
    )(a)


B = 1024


def broadcast(array, axis, root):
    mine = lax.axis_index(axis) == root
    return lax.psum(jnp.where(mine, array, jnp.zeros_like(array)), axis)


def per_device(gradients, ridge, panel_index, block_ids):
    local_rows = gradients.shape[0]
    blocks_here = local_rows // B
    ids = jnp.arange(block_ids.shape[0], dtype=jnp.int32)
    position = jnp.sum(jnp.where(block_ids == panel_index[0], ids, 0))
    owner = position // blocks_here
    offset = position % blocks_here * B
    own_tile = lax.dynamic_slice_in_dim(gradients, offset, B, 0)
    pivot = broadcast(own_tile, "rows", owner)
    numbers = (((1,), (1,)), ((), ()))
    share = local_rows // lax.axis_size("dims")

    rows_n = lax.axis_size("rows")
    core = lax.axis_index("rows") % 2
    half = B // 2
    r_ids = lax.broadcasted_iota(jnp.int32, (half, half), 0)
    c_ids = lax.broadcasted_iota(jnp.int32, (half, half), 1)
    top, bottom = pivot[:half], pivot[half:]

    def lower_left():
        x = _dot_high(bottom, top)
        return jnp.concatenate([x, jnp.zeros((8, half), jnp.float32)], axis=0)

    def diagonal_pair():
        t00 = _dot_high(top, top)
        t11 = _dot_high(bottom, bottom)
        m = jnp.where(r_ids >= c_ids, t00, t11)
        d11 = jnp.sum(jnp.where(r_ids == c_ids, t11, 0.0), axis=0, keepdims=True)
        return jnp.concatenate([m, jnp.broadcast_to(d11, (8, half))], axis=0)

    reduced = lax.psum(lax.cond(core == 0, lower_left, diagonal_pair), "dims")
    swapped = lax.ppermute(reduced, "rows", [(i, i ^ 1) for i in range(rows_n)])
    quarter_x = jnp.where(core == 0, reduced, swapped)[:half]
    packed = jnp.where(core == 0, swapped, reduced)
    m, d11 = packed[:half], packed[half:half + 1]
    t00 = jnp.where(r_ids >= c_ids, m, m.T)
    t11 = jnp.where(r_ids < c_ids, m, jnp.where(r_ids > c_ids, m.T, d11))
    tile = jnp.concatenate(
        [
            jnp.concatenate([t00, jnp.zeros((half, half), jnp.float32)], axis=1),
            jnp.concatenate([quarter_x, t11], axis=1),
        ],
        axis=0,
    )

    column = lax.psum_scatter(
        lax.dot_general(
            gradients,
            pivot,
            numbers,
            precision=lax.Precision.HIGH,
            preferred_element_type=jnp.float32,
        ),
        "dims",
        scatter_dimension=0,
        tiled=True,
    )
    first = lax.axis_index("rows") * local_rows + lax.axis_index("dims") * share
    row_ids = first + jnp.arange(share, dtype=jnp.int32)[:, None]
    col_ids = position * B + jnp.arange(B, dtype=jnp.int32)[None, :]
    column = column + jnp.where(row_ids == col_ids, ridge, jnp.float32(0.0))
    inverse = inv_chol(tile + ridge * jnp.eye(B, dtype=jnp.float32))
    return _dot_high(column, inverse)


def solution(mesh):
    in_specs = (P("rows", "dims"), P(), P(), P())
    out_specs = P(("rows", "dims"), None)
    return jax.shard_map(
        per_device, mesh=mesh, in_specs=in_specs, out_specs=out_specs, check_vma=False
    )
```

```python
import jax
import jax.numpy as jnp
from jax import lax
from jax.experimental import pallas as pl
from jax.experimental.pallas import tpu as pltpu
from jax.sharding import PartitionSpec as P

NB = 128
NPH = 8
HI = lax.Precision.HIGHEST


def _dot_t(a, b):
    return lax.dot_general(a, b, (((1,), (1,)), ((), ())), precision=HI, preferred_element_type=jnp.float32)


def _dot_high(a, b):
    return lax.dot_general(
        a, b, (((1,), (1,)), ((), ())), precision=lax.Precision.HIGH, preferred_element_type=jnp.float32
    )


def _dot(a, b):
    return lax.dot_general(a, b, (((1,), (0,)), ((), ())), precision=HI, preferred_element_type=jnp.float32)


def _factor_block(s):
    sub = NB // NPH
    cid1 = lax.broadcasted_iota(jnp.int32, (1, NB), 1)
    r = jnp.where(lax.broadcasted_iota(jnp.int32, (NB, NB), 0) == lax.broadcasted_iota(jnp.int32, (NB, NB), 1), 1.0, 0.0).astype(jnp.float32)
    done = []
    for p in range(NPH):
        base = p * sub
        rid1 = lax.broadcasted_iota(jnp.int32, (NB - base, 1), 0) + base

        def step(k, carry, rid1=rid1):
            s, r = carry
            row = jnp.sum(jnp.where(rid1 == k, s, 0.0), axis=0, keepdims=True)
            col = jnp.sum(jnp.where(cid1 == k, s, 0.0), axis=1, keepdims=True)
            d = jnp.sum(jnp.where(rid1 == k, col, 0.0), axis=0, keepdims=True)
            inv = lax.rsqrt(d)
            l_row = jnp.where(cid1 >= k, row * inv, 0.0)
            l_col = jnp.where(rid1 >= k, col * inv, 0.0)
            s = s - l_col * l_row
            w_row = jnp.sum(jnp.where(rid1 == k, r, 0.0), axis=0, keepdims=True) * inv
            below = jnp.where(rid1 > k, l_col, 0.0)
            r = jnp.where(rid1 == k, w_row, r - below * w_row)
            return s, r

        s, r = lax.fori_loop(base, base + sub, step, (s, r), unroll=True)
        done.append(r[:sub])
        s, r = s[sub:], r[sub:]
    return jnp.concatenate(done, axis=0)


def _inv_chol_kernel(a_ref, w_ref, work):
    n = a_ref.shape[0]
    nblk = n // NB
    work[...] = a_ref[...]
    w_ref[...] = jnp.zeros_like(w_ref)
    for j in range(nblk):
        o = j * NB
        wjj = _factor_block(work[o:o + NB, o:o + NB])
        w_ref[o:o + NB, o:o + NB] = wjj
        if j < nblk - 1:
            lij = _dot_t(work[o + NB:, o:o + NB], wjj)
            work[o + NB:, o:o + NB] = lij
            work[o + NB:, o + NB:o + 2 * NB] = work[o + NB:, o + NB:o + 2 * NB] - _dot_t(lij, lij[0:NB])
            if j < nblk - 2:
                work[o + 2 * NB:, o + 2 * NB:] = work[o + 2 * NB:, o + 2 * NB:] - _dot_t(lij[NB:], lij[NB:])
        if j > 0:
            t = _dot(work[o:o + NB, 0:o], w_ref[0:o, 0:o])
            w_ref[o:o + NB, 0:o] = -_dot(wjj, t)


def inv_chol(a):
    n = a.shape[0]
    return pl.pallas_call(
        _inv_chol_kernel,
        out_shape=jax.ShapeDtypeStruct((n, n), jnp.float32),
        in_specs=[pl.BlockSpec(memory_space=pltpu.VMEM)],
        out_specs=pl.BlockSpec(memory_space=pltpu.VMEM),
        scratch_shapes=[pltpu.VMEM((n, n), jnp.float32)],
    )(a)


B = 1024


def broadcast(array, axis, root):
    mine = lax.axis_index(axis) == root
    return lax.psum(jnp.where(mine, array, jnp.zeros_like(array)), axis)


def per_device(gradients, ridge, panel_index, block_ids):
    local_rows = gradients.shape[0]
    blocks_here = local_rows // B
    ids = jnp.arange(block_ids.shape[0], dtype=jnp.int32)
    position = jnp.sum(jnp.where(block_ids == panel_index[0], ids, 0))
    owner = position // blocks_here
    offset = position % blocks_here * B
    own_tile = lax.dynamic_slice_in_dim(gradients, offset, B, 0)
    pivot = broadcast(own_tile, "rows", owner)
    numbers = (((1,), (1,)), ((), ()))
    share = local_rows // lax.axis_size("dims")

    rows_n = lax.axis_size("rows")
    core = lax.axis_index("rows") % 2
    half = B // 2
    r_ids = lax.broadcasted_iota(jnp.int32, (half, half), 0)
    c_ids = lax.broadcasted_iota(jnp.int32, (half, half), 1)
    top, bottom = pivot[:half], pivot[half:]

    def lower_left():
        x = _dot_high(bottom, top)
        return jnp.concatenate([x, jnp.zeros((8, half), jnp.float32)], axis=0)

    def diagonal_pair():
        t00 = _dot_high(top, top)
        t11 = _dot_high(bottom, bottom)
        m = jnp.where(r_ids >= c_ids, t00, t11)
        d11 = jnp.sum(jnp.where(r_ids == c_ids, t11, 0.0), axis=0, keepdims=True)
        return jnp.concatenate([m, jnp.broadcast_to(d11, (8, half))], axis=0)

    reduced = lax.psum(lax.cond(core == 0, lower_left, diagonal_pair), "dims")
    swapped = lax.ppermute(reduced, "rows", [(i, i ^ 1) for i in range(rows_n)])
    quarter_x = jnp.where(core == 0, reduced, swapped)[:half]
    packed = jnp.where(core == 0, swapped, reduced)
    m, d11 = packed[:half], packed[half:half + 1]
    t00 = jnp.where(r_ids >= c_ids, m, m.T)
    t11 = jnp.where(r_ids < c_ids, m, jnp.where(r_ids > c_ids, m.T, d11))
    tile = jnp.concatenate(
        [
            jnp.concatenate([t00, jnp.zeros((half, half), jnp.float32)], axis=1),
            jnp.concatenate([quarter_x, t11], axis=1),
        ],
        axis=0,
    )

    column = lax.psum_scatter(
        lax.dot_general(
            gradients,
            pivot,
            numbers,
            precision=lax.Precision.HIGH,
            preferred_element_type=jnp.float32,
        ),
        "dims",
        scatter_dimension=0,
        tiled=True,
    )
    first = lax.axis_index("rows") * local_rows + lax.axis_index("dims") * share
    row_ids = first + jnp.arange(share, dtype=jnp.int32)[:, None]
    col_ids = position * B + jnp.arange(B, dtype=jnp.int32)[None, :]
    column = column + jnp.where(row_ids == col_ids, ridge, jnp.float32(0.0))
    inverse = inv_chol(tile + ridge * jnp.eye(B, dtype=jnp.float32))
    return _dot_high(column, inverse)


def solution(mesh):
    in_specs = (P("rows", "dims"), P(), P(), P())
    out_specs = P(("rows", "dims"), None)
    return jax.shard_map(
        per_device, mesh=mesh, in_specs=in_specs, out_specs=out_specs, check_vma=False
    )
```

```python
import jax
import jax.numpy as jnp
from jax import lax
from jax.experimental import pallas as pl
from jax.experimental.pallas import tpu as pltpu
from jax.sharding import PartitionSpec as P

NB = 128
NPH = 8
HI = lax.Precision.HIGHEST


def _dot_t(a, b):
    return lax.dot_general(a, b, (((1,), (1,)), ((), ())), precision=HI, preferred_element_type=jnp.float32)


def _dot_high(a, b):
    return lax.dot_general(
        a, b, (((1,), (1,)), ((), ())), precision=lax.Precision.HIGH, preferred_element_type=jnp.float32
    )


def _dot(a, b):
    return lax.dot_general(a, b, (((1,), (0,)), ((), ())), precision=HI, preferred_element_type=jnp.float32)


def _factor_block(s):
    sub = NB // NPH
    cid1 = lax.broadcasted_iota(jnp.int32, (1, NB), 1)
    r = jnp.where(lax.broadcasted_iota(jnp.int32, (NB, NB), 0) == lax.broadcasted_iota(jnp.int32, (NB, NB), 1), 1.0, 0.0).astype(jnp.float32)
    done = []
    for p in range(NPH):
        base = p * sub
        rid1 = lax.broadcasted_iota(jnp.int32, (NB - base, 1), 0) + base

        def step(k, carry, rid1=rid1):
            s, r = carry
            row = jnp.sum(jnp.where(rid1 == k, s, 0.0), axis=0, keepdims=True)
            col = jnp.sum(jnp.where(cid1 == k, s, 0.0), axis=1, keepdims=True)
            d = jnp.sum(jnp.where(rid1 == k, col, 0.0), axis=0, keepdims=True)
            inv = lax.rsqrt(d)
            l_row = jnp.where(cid1 >= k, row * inv, 0.0)
            l_col = jnp.where(rid1 >= k, col * inv, 0.0)
            s = s - l_col * l_row
            w_row = jnp.sum(jnp.where(rid1 == k, r, 0.0), axis=0, keepdims=True) * inv
            below = jnp.where(rid1 > k, l_col, 0.0)
            r = jnp.where(rid1 == k, w_row, r - below * w_row)
            return s, r

        s, r = lax.fori_loop(base, base + sub, step, (s, r), unroll=True)
        done.append(r[:sub])
        s, r = s[sub:], r[sub:]
    return jnp.concatenate(done, axis=0)


def _inv_chol_kernel(x_ref, m_ref, ridge_ref, w_ref, work):
    n = w_ref.shape[0]
    nblk = n // NB
    half = n // 2
    r_ids = lax.broadcasted_iota(jnp.int32, (half, half), 0)
    c_ids = lax.broadcasted_iota(jnp.int32, (half, half), 1)
    m = m_ref[0:half, :]
    mt = m.T
    ridge = ridge_ref[0, 0]
    diag = jnp.where(r_ids == c_ids, ridge, 0.0)
    d11 = m_ref[half:half + 1, :]
    work[0:half, 0:half] = jnp.where(r_ids >= c_ids, m, mt) + diag
    work[0:half, half:n] = jnp.zeros((half, half), jnp.float32)
    work[half:n, 0:half] = x_ref[0:half, :]
    work[half:n, half:n] = jnp.where(r_ids < c_ids, m, jnp.where(r_ids > c_ids, mt, d11)) + diag
    w_ref[...] = jnp.zeros_like(w_ref)
    for j in range(nblk):
        o = j * NB
        wjj = _factor_block(work[o:o + NB, o:o + NB])
        w_ref[o:o + NB, o:o + NB] = wjj
        if j < nblk - 1:
            lij = _dot_t(work[o + NB:, o:o + NB], wjj)
            work[o + NB:, o:o + NB] = lij
            work[o + NB:, o + NB:o + 2 * NB] = work[o + NB:, o + NB:o + 2 * NB] - _dot_t(lij, lij[0:NB])
            if j < nblk - 2:
                work[o + 2 * NB:, o + 2 * NB:] = work[o + 2 * NB:, o + 2 * NB:] - _dot_t(lij[NB:], lij[NB:])
        if j > 0:
            t = _dot(work[o:o + NB, 0:o], w_ref[0:o, 0:o])
            w_ref[o:o + NB, 0:o] = -_dot(wjj, t)


def inv_chol(quarter_x, packed, ridge):
    n = 2 * quarter_x.shape[1]
    return pl.pallas_call(
        _inv_chol_kernel,
        out_shape=jax.ShapeDtypeStruct((n, n), jnp.float32),
        in_specs=[
            pl.BlockSpec(memory_space=pltpu.VMEM),
            pl.BlockSpec(memory_space=pltpu.VMEM),
            pl.BlockSpec(memory_space=pltpu.SMEM),
        ],
        out_specs=pl.BlockSpec(memory_space=pltpu.VMEM),
        scratch_shapes=[pltpu.VMEM((n, n), jnp.float32)],
    )(quarter_x, packed, ridge.reshape(1, 1))


B = 1024


def broadcast(array, axis, root):
    mine = lax.axis_index(axis) == root
    return lax.psum(jnp.where(mine, array, jnp.zeros_like(array)), axis)


def per_device(gradients, ridge, panel_index, block_ids):
    local_rows = gradients.shape[0]
    blocks_here = local_rows // B
    ids = jnp.arange(block_ids.shape[0], dtype=jnp.int32)
    position = jnp.sum(jnp.where(block_ids == panel_index[0], ids, 0))
    owner = position // blocks_here
    offset = position % blocks_here * B
    own_tile = lax.dynamic_slice_in_dim(gradients, offset, B, 0)
    pivot = broadcast(own_tile, "rows", owner)
    numbers = (((1,), (1,)), ((), ()))
    share = local_rows // lax.axis_size("dims")

    rows_n = lax.axis_size("rows")
    core = lax.axis_index("rows") % 2
    half = B // 2
    r_ids = lax.broadcasted_iota(jnp.int32, (half, half), 0)
    c_ids = lax.broadcasted_iota(jnp.int32, (half, half), 1)
    top, bottom = pivot[:half], pivot[half:]

    def lower_left():
        x = _dot_high(bottom, top)
        return jnp.concatenate([x, jnp.zeros((8, half), jnp.float32)], axis=0)

    def diagonal_pair():
        t00 = _dot_high(top, top)
        t11 = _dot_high(bottom, bottom)
        m = jnp.where(r_ids >= c_ids, t00, t11)
        d11 = jnp.sum(jnp.where(r_ids == c_ids, t11, 0.0), axis=0, keepdims=True)
        return jnp.concatenate([m, jnp.broadcast_to(d11, (8, half))], axis=0)

    reduced = lax.psum(lax.cond(core == 0, lower_left, diagonal_pair), "dims")
    swapped = lax.ppermute(reduced, "rows", [(i, i ^ 1) for i in range(rows_n)])
    quarter_x = jnp.where(core == 0, reduced, swapped)
    packed = jnp.where(core == 0, swapped, reduced)

    column = lax.psum_scatter(
        lax.dot_general(
            gradients,
            pivot,
            numbers,
            precision=lax.Precision.HIGH,
            preferred_element_type=jnp.float32,
        ),
        "dims",
        scatter_dimension=0,
        tiled=True,
    )
    first = lax.axis_index("rows") * local_rows + lax.axis_index("dims") * share
    row_ids = first + jnp.arange(share, dtype=jnp.int32)[:, None]
    col_ids = position * B + jnp.arange(B, dtype=jnp.int32)[None, :]
    column = column + jnp.where(row_ids == col_ids, ridge, jnp.float32(0.0))
    inverse = inv_chol(quarter_x, packed, ridge)
    return _dot_high(column, inverse)


def solution(mesh):
    in_specs = (P("rows", "dims"), P(), P(), P())
    out_specs = P(("rows", "dims"), None)
    return jax.shard_map(
        per_device, mesh=mesh, in_specs=in_specs, out_specs=out_specs, check_vma=False
    )
```

```python
import jax
import jax.numpy as jnp
from jax import lax
from jax.experimental import pallas as pl
from jax.experimental.pallas import tpu as pltpu
from jax.sharding import PartitionSpec as P

NB = 128
NPH = 8
HI = lax.Precision.HIGHEST


def _dot_t(a, b):
    return lax.dot_general(a, b, (((1,), (1,)), ((), ())), precision=HI, preferred_element_type=jnp.float32)


def _dot_high(a, b):
    return lax.dot_general(
        a, b, (((1,), (1,)), ((), ())), precision=lax.Precision.HIGH, preferred_element_type=jnp.float32
    )


def _dot(a, b):
    return lax.dot_general(a, b, (((1,), (0,)), ((), ())), precision=HI, preferred_element_type=jnp.float32)


def _factor_block(s):
    sub = NB // NPH
    cid1 = lax.broadcasted_iota(jnp.int32, (1, NB), 1)
    r = jnp.where(lax.broadcasted_iota(jnp.int32, (NB, NB), 0) == lax.broadcasted_iota(jnp.int32, (NB, NB), 1), 1.0, 0.0).astype(jnp.float32)
    done = []
    for p in range(NPH):
        base = p * sub
        rid1 = lax.broadcasted_iota(jnp.int32, (NB - base, 1), 0) + base

        def step(k, carry, rid1=rid1):
            s, r = carry
            row = jnp.sum(jnp.where(rid1 == k, s, 0.0), axis=0, keepdims=True)
            col = jnp.sum(jnp.where(cid1 == k, s, 0.0), axis=1, keepdims=True)
            d = jnp.sum(jnp.where(rid1 == k, col, 0.0), axis=0, keepdims=True)
            inv = lax.rsqrt(d)
            l_row = jnp.where(cid1 >= k, row * inv, 0.0)
            l_col = jnp.where(rid1 >= k, col * inv, 0.0)
            s = s - l_col * l_row
            w_row = jnp.sum(jnp.where(rid1 == k, r, 0.0), axis=0, keepdims=True) * inv
            below = jnp.where(rid1 > k, l_col, 0.0)
            r = jnp.where(rid1 == k, w_row, r - below * w_row)
            return s, r

        s, r = lax.fori_loop(base, base + sub, step, (s, r), unroll=True)
        done.append(r[:sub])
        s, r = s[sub:], r[sub:]
    return jnp.concatenate(done, axis=0)


def _inv_chol_kernel(x_ref, m_ref, ridge_ref, w_ref, work):
    n = w_ref.shape[0]
    nblk = n // NB
    half = n // 2
    r_ids = lax.broadcasted_iota(jnp.int32, (half, half), 0)
    c_ids = lax.broadcasted_iota(jnp.int32, (half, half), 1)
    m = m_ref[0:half, :]
    mt = m.T
    ridge = ridge_ref[0, 0]
    diag = jnp.where(r_ids == c_ids, ridge, 0.0)
    d11 = m_ref[half:half + 1, :]
    work[0:half, 0:half] = jnp.where(r_ids >= c_ids, m, mt) + diag
    work[0:half, half:n] = jnp.zeros((half, half), jnp.float32)
    work[half:n, 0:half] = x_ref[0:half, :]
    work[half:n, half:n] = jnp.where(r_ids < c_ids, m, jnp.where(r_ids > c_ids, mt, d11)) + diag
    w_ref[...] = jnp.zeros_like(w_ref)
    for j in range(nblk):
        o = j * NB
        wjj = _factor_block(work[o:o + NB, o:o + NB])
        w_ref[o:o + NB, o:o + NB] = wjj
        if j < nblk - 1:
            lij = _dot_t(work[o + NB:, o:o + NB], wjj)
            work[o + NB:, o:o + NB] = lij
            work[o + NB:, o + NB:o + 2 * NB] = work[o + NB:, o + NB:o + 2 * NB] - _dot_t(lij, lij[0:NB])
            if j < nblk - 2:
                work[o + 2 * NB:, o + 2 * NB:] = work[o + 2 * NB:, o + 2 * NB:] - _dot_t(lij[NB:], lij[NB:])
        if j > 0:
            t = _dot(work[o:o + NB, 0:o], w_ref[0:o, 0:o])
            w_ref[o:o + NB, 0:o] = -_dot(wjj, t)


def inv_chol(quarter_x, packed, ridge):
    n = 2 * quarter_x.shape[1]
    return pl.pallas_call(
        _inv_chol_kernel,
        out_shape=jax.ShapeDtypeStruct((n, n), jnp.float32),
        in_specs=[
            pl.BlockSpec(memory_space=pltpu.VMEM),
            pl.BlockSpec(memory_space=pltpu.VMEM),
            pl.BlockSpec(memory_space=pltpu.SMEM),
        ],
        out_specs=pl.BlockSpec(memory_space=pltpu.VMEM),
        scratch_shapes=[pltpu.VMEM((n, n), jnp.float32)],
    )(quarter_x, packed, ridge.reshape(1, 1))


B = 1024


def broadcast(array, axis, root):
    mine = lax.axis_index(axis) == root
    return lax.psum(jnp.where(mine, array, jnp.zeros_like(array)), axis)


def per_device(gradients, ridge, panel_index, block_ids):
    local_rows = gradients.shape[0]
    blocks_here = local_rows // B
    ids = jnp.arange(block_ids.shape[0], dtype=jnp.int32)
    position = jnp.sum(jnp.where(block_ids == panel_index[0], ids, 0))
    owner = position // blocks_here
    offset = position % blocks_here * B
    own_tile = lax.dynamic_slice_in_dim(gradients, offset, B, 0)
    pivot = broadcast(own_tile, "rows", owner)
    numbers = (((1,), (1,)), ((), ()))
    share = local_rows // lax.axis_size("dims")

    rows_n = lax.axis_size("rows")
    core = lax.axis_index("rows") % 2
    half = B // 2
    r_ids = lax.broadcasted_iota(jnp.int32, (half, half), 0)
    c_ids = lax.broadcasted_iota(jnp.int32, (half, half), 1)
    top, bottom = pivot[:half], pivot[half:]

    def lower_left():
        x = _dot_high(bottom, top)
        return jnp.concatenate([x, jnp.zeros((8, half), jnp.float32)], axis=0)

    def diagonal_pair():
        t00 = _dot_high(top, top)
        t11 = _dot_high(bottom, bottom)
        m = jnp.where(r_ids >= c_ids, t00, t11)
        d11 = jnp.sum(jnp.where(r_ids == c_ids, t11, 0.0), axis=0, keepdims=True)
        return jnp.concatenate([m, jnp.broadcast_to(d11, (8, half))], axis=0)

    reduced = lax.psum(lax.cond(core == 0, lower_left, diagonal_pair), "dims")
    swapped = lax.ppermute(reduced, "rows", [(i, i ^ 1) for i in range(rows_n)])
    quarter_x = jnp.where(core == 0, reduced, swapped)
    packed = jnp.where(core == 0, swapped, reduced)

    column = lax.psum_scatter(
        lax.dot_general(
            gradients,
            pivot,
            numbers,
            precision=lax.Precision.HIGH,
            preferred_element_type=jnp.float32,
        ),
        "dims",
        scatter_dimension=0,
        tiled=True,
    )
    first = lax.axis_index("rows") * local_rows + lax.axis_index("dims") * share
    row_ids = first + jnp.arange(share, dtype=jnp.int32)[:, None]
    col_ids = position * B + jnp.arange(B, dtype=jnp.int32)[None, :]
    column = column + jnp.where(row_ids == col_ids, ridge, jnp.float32(0.0))
    inverse = inv_chol(quarter_x, packed, ridge)
    return jnp.concatenate(
        [_dot_high(column[:, :half], inverse[:half, :half]), _dot_high(column, inverse[half:])],
        axis=1,
    )


def solution(mesh):
    in_specs = (P("rows", "dims"), P(), P(), P())
    out_specs = P(("rows", "dims"), None)
    return jax.shard_map(
        per_device, mesh=mesh, in_specs=in_specs, out_specs=out_specs, check_vma=False
    )
```

```python
import jax
import jax.numpy as jnp
from jax import lax
from jax.experimental import pallas as pl
from jax.experimental.pallas import tpu as pltpu
from jax.sharding import PartitionSpec as P

NB = 128
NPH = 8
HI = lax.Precision.HIGHEST


def _dot_t(a, b):
    return lax.dot_general(a, b, (((1,), (1,)), ((), ())), precision=HI, preferred_element_type=jnp.float32)


def _dot_high(a, b):
    return lax.dot_general(
        a, b, (((1,), (1,)), ((), ())), precision=lax.Precision.HIGH, preferred_element_type=jnp.float32
    )


def _dot(a, b):
    return lax.dot_general(a, b, (((1,), (0,)), ((), ())), precision=HI, preferred_element_type=jnp.float32)


def _factor_block(s):
    sub = NB // NPH
    cid1 = lax.broadcasted_iota(jnp.int32, (1, NB), 1)
    r = jnp.where(lax.broadcasted_iota(jnp.int32, (NB, NB), 0) == lax.broadcasted_iota(jnp.int32, (NB, NB), 1), 1.0, 0.0).astype(jnp.float32)
    done = []
    for p in range(NPH):
        base = p * sub
        rid1 = lax.broadcasted_iota(jnp.int32, (NB - base, 1), 0) + base

        def step(k, carry, rid1=rid1):
            s, r = carry
            row = jnp.sum(jnp.where(rid1 == k, s, 0.0), axis=0, keepdims=True)
            col = jnp.sum(jnp.where(cid1 == k, s, 0.0), axis=1, keepdims=True)
            d = jnp.sum(jnp.where(rid1 == k, col, 0.0), axis=0, keepdims=True)
            inv = lax.rsqrt(d)
            l_row = jnp.where(cid1 >= k, row * inv, 0.0)
            l_col = jnp.where(rid1 >= k, col * inv, 0.0)
            s = s - l_col * l_row
            w_row = jnp.sum(jnp.where(rid1 == k, r, 0.0), axis=0, keepdims=True) * inv
            below = jnp.where(rid1 > k, l_col, 0.0)
            r = jnp.where(rid1 == k, w_row, r - below * w_row)
            return s, r

        s, r = lax.fori_loop(base, base + sub, step, (s, r), unroll=True)
        done.append(r[:sub])
        s, r = s[sub:], r[sub:]
    return jnp.concatenate(done, axis=0)


def _inv_chol_kernel(x_ref, m_ref, ridge_ref, w_ref, work):
    n = w_ref.shape[0]
    nblk = n // NB
    half = n // 2
    r_ids = lax.broadcasted_iota(jnp.int32, (half, half), 0)
    c_ids = lax.broadcasted_iota(jnp.int32, (half, half), 1)
    m = m_ref[0:half, :]
    mt = m.T
    ridge = ridge_ref[0, 0]
    diag = jnp.where(r_ids == c_ids, ridge, 0.0)
    d11 = m_ref[half:half + 1, :]
    work[0:half, 0:half] = jnp.where(r_ids >= c_ids, m, mt) + diag
    work[0:half, half:n] = jnp.zeros((half, half), jnp.float32)
    work[half:n, 0:half] = x_ref[0:half, :]
    work[half:n, half:n] = jnp.where(r_ids < c_ids, m, jnp.where(r_ids > c_ids, mt, d11)) + diag
    w_ref[...] = jnp.zeros_like(w_ref)
    for j in range(nblk):
        o = j * NB
        wjj = _factor_block(work[o:o + NB, o:o + NB])
        w_ref[o:o + NB, o:o + NB] = wjj
        if j < nblk - 1:
            lij = _dot_t(work[o + NB:, o:o + NB], wjj)
            work[o + NB:, o:o + NB] = lij
            work[o + NB:, o + NB:o + 2 * NB] = work[o + NB:, o + NB:o + 2 * NB] - _dot_t(lij, lij[0:NB])
            if j < nblk - 2:
                work[o + 2 * NB:, o + 2 * NB:] = work[o + 2 * NB:, o + 2 * NB:] - _dot_t(lij[NB:], lij[NB:])
        if j > 0:
            t = _dot(work[o:o + NB, 0:o], w_ref[0:o, 0:o])
            w_ref[o:o + NB, 0:o] = -_dot(wjj, t)


def inv_chol(quarter_x, packed, ridge):
    n = 2 * quarter_x.shape[1]
    return pl.pallas_call(
        _inv_chol_kernel,
        out_shape=jax.ShapeDtypeStruct((n, n), jnp.float32),
        in_specs=[
            pl.BlockSpec(memory_space=pltpu.VMEM),
            pl.BlockSpec(memory_space=pltpu.VMEM),
            pl.BlockSpec(memory_space=pltpu.SMEM),
        ],
        out_specs=pl.BlockSpec(memory_space=pltpu.VMEM),
        scratch_shapes=[pltpu.VMEM((n, n), jnp.float32)],
    )(quarter_x, packed, ridge.reshape(1, 1))


B = 1024


def broadcast(array, axis, root):
    mine = lax.axis_index(axis) == root
    return lax.psum(jnp.where(mine, array, jnp.zeros_like(array)), axis)


def per_device(gradients, ridge, panel_index, block_ids):
    local_rows = gradients.shape[0]
    blocks_here = local_rows // B
    ids = jnp.arange(block_ids.shape[0], dtype=jnp.int32)
    position = jnp.sum(jnp.where(block_ids == panel_index[0], ids, 0))
    owner = position // blocks_here
    offset = position % blocks_here * B
    own_tile = lax.dynamic_slice_in_dim(gradients, offset, B, 0)
    pivot = broadcast(own_tile, "rows", owner)
    numbers = (((1,), (1,)), ((), ()))
    share = local_rows // lax.axis_size("dims")

    rows_n = lax.axis_size("rows")
    core = lax.axis_index("rows") % 2
    half = B // 2
    r_ids = lax.broadcasted_iota(jnp.int32, (half, half), 0)
    c_ids = lax.broadcasted_iota(jnp.int32, (half, half), 1)
    top, bottom = pivot[:half], pivot[half:]

    def lower_left():
        x = _dot_high(bottom, top)
        return jnp.concatenate([x, jnp.zeros((8, half), jnp.float32)], axis=0)

    def diagonal_pair():
        t00 = _dot_high(top, top)
        t11 = _dot_high(bottom, bottom)
        m = jnp.where(r_ids >= c_ids, t00, t11)
        d11 = jnp.sum(jnp.where(r_ids == c_ids, t11, 0.0), axis=0, keepdims=True)
        return jnp.concatenate([m, jnp.broadcast_to(d11, (8, half))], axis=0)

    reduced = lax.psum(lax.cond(core == 0, lower_left, diagonal_pair), "dims")
    swapped = lax.ppermute(reduced, "rows", [(i, i ^ 1) for i in range(rows_n)])
    quarter_x = jnp.where(core == 0, reduced, swapped)
    packed = jnp.where(core == 0, swapped, reduced)

    column = lax.psum_scatter(
        lax.dot_general(
            gradients,
            pivot,
            numbers,
            precision=lax.Precision.HIGH,
            preferred_element_type=jnp.float32,
        ),
        "dims",
        scatter_dimension=0,
        tiled=True,
    )
    first = lax.axis_index("rows") * local_rows + lax.axis_index("dims") * share
    row_ids = first + jnp.arange(share, dtype=jnp.int32)[:, None]
    col_ids = position * B + jnp.arange(B, dtype=jnp.int32)[None, :]
    column = column + jnp.where(row_ids == col_ids, ridge, jnp.float32(0.0))
    inverse = inv_chol(quarter_x, packed, ridge)
    q = B // 4
    return jnp.concatenate(
        [_dot_high(column[:, :(i + 1) * q], inverse[i * q:(i + 1) * q, :(i + 1) * q]) for i in range(4)],
        axis=1,
    )


def solution(mesh):
    in_specs = (P("rows", "dims"), P(), P(), P())
    out_specs = P(("rows", "dims"), None)
    return jax.shard_map(
        per_device, mesh=mesh, in_specs=in_specs, out_specs=out_specs, check_vma=False
    )
```
